32 devices in a mesh: row: 2 (over x), col: 4 (over z), tok: 4 (over y, core).
Axes of the slice: x: 2, y: 2, z: 4, core: 2. Of those that a mesh axis runs over, the one named last changes fastest.
Arguments:
- activations: bfloat16 [4096, 2048], P(('row', 'col', 'tok')), may hold values from -6 to 6
- norm_gain: float32 [2048], replicated, may hold values from 0.1 to 1.9
- routes: int32 [4096, 8], P(('row', 'col', 'tok')), may hold values from 0 to 127, all different within a row; in each aligned block of 128 rows (0 to 127, 128 to 255, ...) at most 10 rows name the same one
- route_weights: float32 [4096, 8], P(('row', 'col', 'tok')), may hold values from 0.05 to 1
- gate_up_weight: bfloat16 [128, 2, 768, 2048], P(('row', 'col'), None, 'tok'), may hold values from -0.125 to 0.125
- down_weight: bfloat16 [128, 768, 2048], P(('row', 'col'), 'tok'), may hold values from -0.21875 to 0.21875
Outputs:
- expert_mix: bfloat16 [4096, 2048], P(('row', 'col', 'tok'))
The draws below stay inside these ranges and needn't reach their ends.
Inputs may be any that keep to these rules, and one draw needn't show every extreme that they name: `routes`: within the rows of one device no expert is named by more than 10 rows, a bound that some block reaches.
All inputs are finite; a program needn't handle non-finite values.
Results may differ from the reference program's by a relative error of at most 0.0085.
Values may be sent and summed in bfloat16 or wider, within the bound.
No kernel may reach another device: no remote copies, remote signals or barrier semaphores. Data moves between devices by JAX's collectives and lax.ppermute only.
A program may use at most 384 MiB of HBM per device.

```python
import math
import jax
import jax.numpy as jnp
import numpy as np
from jax import lax

D = 2048
FF = 768
EXPERTS = 128
TOP = 8
TOK_DEV = 128
CAP = 10
TOKENS = 4096


def shard_levels(rng, dims, shards, low, top_value):
    factor_of = 1.0
    for dim, parts in shards:
        draws = jax.random.uniform(jax.random.fold_in(jax.random.fold_in(rng, 6), dim), (parts,), jnp.float32, low / len(shards), top_value / len(shards))
        factor_of = factor_of * jnp.repeat(jnp.exp(draws), dims[dim] // parts).reshape((-1,) + (1,) * (len(dims) - 1 - dim))
    return factor_of


def assign_block(stream_key, own, number, rows, number_of, top, reach, slope):
    sequence = jax.random.permutation(stream_key, number_of)
    heavy_load, common = shares(number_of, rows * top, reach, slope, True), shares(number_of, rows * top, reach, slope, False)
    places = jnp.arange(number_of)

    def named(tallies, rotation):
        used = int((tallies > 0).sum())
        fixed = max(1, used // 4)
        passed = fixed + (places - fixed + rotation * (used - fixed)) % max(1, number_of - fixed)
        return jnp.zeros((number_of,), jnp.int32).at[sequence[jnp.where(places < fixed, places, passed)]].set(jnp.asarray(tallies, jnp.int32))

    tallies = jnp.where(number % 4 == 0, named(heavy_load, number // 4), named(common, number - number // 4 - 1))
    mixed = jax.random.permutation(jax.random.fold_in(own, 3), number_of)
    source_of, receiver = mixed[0:number_of // 2 * 2:2], mixed[1:number_of // 2 * 2:2]
    margin = jnp.minimum(tallies[source_of] - 1, reach - tallies[receiver]) // 2
    margin = jnp.where((source_of == sequence[0]) | (receiver == sequence[0]) | (tallies[receiver] == 0), 0, jnp.maximum(margin, 0))
    passed = jax.random.randint(jax.random.fold_in(own, 4), (number_of // 2,), 0, 1 << 20) % (margin + 1)
    tallies = tallies.at[source_of].add(-passed).at[receiver].add(passed)
    members = jnp.searchsorted(jnp.cumsum(tallies), jnp.arange(rows * top), side="right").astype(jnp.int32)
    listing = members.reshape(top, rows).T
    listing = listing[jax.random.permutation(jax.random.fold_in(own, 1), rows)]
    rotation = jax.random.randint(jax.random.fold_in(own, 2), (rows, 1), 0, top)
    return jnp.take_along_axis(listing, (jnp.arange(top)[None, :] + rotation) % top, axis=1)


def shares(number_of, total, most, skew, full):
    loads = [(1 << 20) // math.isqrt(rank ** skew) + 1 for rank in range(1, number_of + 1)]
    largest = most if full else min(most, max(-(-total // number_of), total * loads[0] // sum(loads)))
    least = 1 if total - largest >= number_of - 1 else 0
    given, spare = [largest] + [least] * (number_of - 1), total - largest - least * (number_of - 1)
    while spare > 0:
        movable = [i for i in range(1, number_of) if given[i] < largest] or [i for i in range(1, number_of) if given[i] < most]
        whole, left = sum([loads[i] for i in movable]), spare
        for i in movable:
            addition = min(most - given[i], max(1, left * loads[i] // whole), spare)
            given[i] = given[i] + addition
            spare = spare - addition
    return np.array(given)


def centred(stream_key, shape, spread, bound, pieces=(), held_as=jnp.bfloat16):
    loudness = shard_levels(stream_key, shape, pieces, -0.22, 0.18) if pieces else 1.0
    values = jax.random.normal(stream_key, shape, jnp.float32) * spread * loudness
    return jnp.minimum(jnp.maximum(values, -bound), bound).astype(held_as)


def setup_inputs(seed: int = 0) -> dict:
    streams_of = jax.random.split(jax.random.key(seed), 7)
    activations = centred(streams_of[0], (TOKENS, D), 1.0, 6.0, ((0, 32),))
    norm_gain = jnp.clip(1.0 + 0.18 * jax.random.normal(streams_of[1], (D,), jnp.float32), 0.1, 1.9)
    routes_keys = jax.random.split(jax.random.fold_in(streams_of[2], 1), TOKENS // TOK_DEV)
    routes_turns = jax.random.permutation(jax.random.fold_in(streams_of[2], 3), TOKENS // TOK_DEV)
    routes = jax.vmap(lambda own, number: assign_block(jax.random.fold_in(streams_of[2], 2), own, number, TOK_DEV, EXPERTS, TOP, CAP, 1))(routes_keys, routes_turns).reshape((TOKENS, TOP))
    route_weights = jnp.clip(jnp.exp(math.log(1.0) - 2.9957323 * jax.random.uniform(streams_of[3], (TOKENS, TOP), jnp.float32) ** shard_levels(streams_of[3], (TOKENS, TOP), ((0, 32),), -0.2, 0.2)), 0.05, 1.0)
    gate_up_weight = centred(streams_of[4], (EXPERTS, 2, FF, D), D ** -0.5, 0.125, ((0, 8), (2, 4)))
    down_weight = centred(streams_of[5], (EXPERTS, FF, D), FF ** -0.5, 0.21875, ((0, 8), (1, 4)))
    return {"activations": activations, "norm_gain": norm_gain, "routes": routes, "route_weights": route_weights, "gate_up_weight": gate_up_weight, "down_weight": down_weight}


EPSILON = 1e-06

def rank_in_block(block_routes):
    onehot = (block_routes[:, None] == jnp.arange(EXPERTS, dtype=jnp.int32)[None, :]).astype(jnp.int32)
    before = jnp.cumsum(onehot, axis=0) - onehot
    return lax.optimization_barrier(jnp.sum(before * onehot, axis=1)).astype(jnp.int32)

def reference(activations, norm_gain, routes, route_weights, gate_up_weight, down_weight):
    values = activations.astype(jnp.float32)
    scale = lax.rsqrt(lax.optimization_barrier(jnp.mean(values * values, axis=-1, keepdims=True)) + EPSILON)
    normed = (values * scale * norm_gain).astype(jnp.bfloat16)
    gates = route_weights / lax.optimization_barrier(jnp.sum(route_weights, axis=1, keepdims=True))
    blocks = TOKENS // TOK_DEV
    pairs = TOK_DEV * TOP
    ranks = lax.map(rank_in_block, routes.reshape(blocks, pairs)).reshape(-1).astype(jnp.int32)
    flat_routes = routes.reshape(-1).astype(jnp.int32)
    pair_ids = jnp.arange(TOKENS * TOP, dtype=jnp.int32)
    block_ids = pair_ids // pairs
    per_expert = blocks * CAP
    slots = flat_routes * per_expert + block_ids * CAP + ranks
    token_ids = pair_ids // TOP
    table = jnp.full((EXPERTS * per_expert,), TOKENS, jnp.int32).at[slots].set(token_ids)
    weight_table = jnp.zeros((EXPERTS * per_expert,), jnp.float32).at[slots].set(gates.reshape(-1))
    table = table.reshape(EXPERTS, per_expert)
    weight_table = weight_table.reshape(EXPERTS, per_expert)
    padded = jnp.concatenate([normed, jnp.zeros((1, D), jnp.bfloat16)], axis=0)

    def one_expert(total, item):
        index, weights, gate_up, down = item
        picked = padded[index]
        gate = jnp.dot(picked, gate_up[0].T, preferred_element_type=jnp.float32)
        upward = jnp.dot(picked, gate_up[1].T, preferred_element_type=jnp.float32)
        hidden = (jax.nn.silu(gate) * upward).astype(jnp.bfloat16)
        output = jnp.dot(hidden, down, preferred_element_type=jnp.float32).astype(jnp.bfloat16)
        total = total.at[index].add(weights[:, None] * output.astype(jnp.float32))
        return (total, None)
    start_total = jnp.zeros((TOKENS + 1, D), jnp.float32)
    total, _ = lax.scan(one_expert, start_total, (table, weight_table, gate_up_weight, down_weight))
    return total[:TOKENS].astype(jnp.bfloat16)
```

```python
import jax
import jax.numpy as jnp
from jax import lax
from jax.sharding import PartitionSpec as P

CAP = 10


EPSILON = 1e-06

ALL = ("row", "col", "tok")


def rank_in_block(block_routes, experts):
    onehot = (block_routes[:, None] == jnp.arange(experts, dtype=jnp.int32)[None, :]).astype(
        jnp.int32
    )
    before = jnp.cumsum(onehot, axis=0) - onehot
    return jnp.sum(before * onehot, axis=1)


def rms_normed(activations, norm_gain):
    values = activations.astype(jnp.float32)
    scale = lax.rsqrt(jnp.mean(values * values, axis=-1, keepdims=True) + EPSILON)
    return (values * scale * norm_gain).astype(jnp.bfloat16)


def local(activations, norm_gain, routes, route_weights, gate_up_weight, down_weight):
    count, features = activations.shape
    chosen = routes.shape[1]
    holding = gate_up_weight.shape[0]
    row_count = lax.axis_size("row")
    col_count = lax.axis_size("col")
    tok_count = lax.axis_size("tok")
    owners = row_count * col_count
    experts = holding * owners
    devices = owners * tok_count
    owner = lax.axis_index("row") * col_count + lax.axis_index("col")

    normed = rms_normed(activations, norm_gain)
    gates = route_weights / jnp.sum(route_weights, axis=1, keepdims=True)
    flat_routes = routes.reshape(-1)
    target = flat_routes * CAP + rank_in_block(flat_routes, experts)

    every_normed = lax.all_gather(normed, ALL, axis=0, tiled=True)
    every_target = lax.all_gather(target, ALL, axis=0, tiled=False)

    source = jnp.arange(devices, dtype=jnp.int32)[:, None]
    pair = jnp.arange(count * chosen, dtype=jnp.int32)[None, :]
    expert = every_target // CAP
    rank = every_target % CAP
    mine = expert // holding == owner
    slot = (
        ((source % tok_count) * owners + source // tok_count) * holding + expert % holding
    ) * CAP + rank
    slots = tok_count * owners * holding * CAP
    slot = jnp.where(mine, slot, slots)
    token = source * count + pair // chosen
    table = jnp.full((slots,), devices * count, jnp.int32).at[slot.reshape(-1)].set(
        token.reshape(-1), mode="drop"
    )
    picked = jnp.take(every_normed, table, axis=0, mode="fill", fill_value=0)
    picked = picked.reshape(tok_count * owners, holding, CAP, features)

    both = jnp.einsum(
        "sjcd,jgfd->sjcgf", picked, gate_up_weight, preferred_element_type=jnp.float32
    )
    hidden = (jax.nn.silu(both[:, :, :, 0, :]) * both[:, :, :, 1, :]).astype(jnp.bfloat16)
    partial = jnp.einsum(
        "sjcf,jfd->sjcd", hidden, down_weight, preferred_element_type=jnp.float32
    )
    summed = lax.psum_scatter(partial, "tok", scatter_dimension=0, tiled=True)
    results = summed.astype(jnp.bfloat16)

    returned = lax.all_to_all(results, ("row", "col"), split_axis=0, concat_axis=0, tiled=True)
    picked_back = jnp.take(returned.reshape(experts * CAP, features), target, axis=0)
    picked_back = picked_back.reshape(count, chosen, features)
    mixed = jnp.einsum("tk,tkd->td", gates, picked_back.astype(jnp.float32))
    return mixed.astype(jnp.bfloat16)


def solution(mesh):
    in_specs = (
        P(("row", "col", "tok"), None),
        P(),
        P(("row", "col", "tok"), None),
        P(("row", "col", "tok"), None),
        P(("row", "col"), None, "tok", None),
        P(("row", "col"), "tok", None),
    )
    out_specs = P(("row", "col", "tok"), None)
    return jax.shard_map(local, mesh=mesh, in_specs=in_specs, out_specs=out_specs, check_vma=False)
```

```python
import jax
import jax.numpy as jnp
from jax import lax
from jax.sharding import PartitionSpec as P

CAP = 10


EPSILON = 1e-06

ALL = ("row", "col", "tok")


def rank_in_block(block_routes, experts):
    onehot = (block_routes[:, None] == jnp.arange(experts, dtype=jnp.int32)[None, :]).astype(
        jnp.int32
    )
    before = jnp.cumsum(onehot, axis=0) - onehot
    return jnp.sum(before * onehot, axis=1)


def rms_normed(activations, norm_gain):
    values = activations.astype(jnp.float32)
    scale = lax.rsqrt(jnp.mean(values * values, axis=-1, keepdims=True) + EPSILON)
    return (values * scale * norm_gain).astype(jnp.bfloat16)


def local(activations, norm_gain, routes, route_weights, gate_up_weight, down_weight):
    count, features = activations.shape
    chosen = routes.shape[1]
    holding = gate_up_weight.shape[0]
    row_count = lax.axis_size("row")
    col_count = lax.axis_size("col")
    tok_count = lax.axis_size("tok")
    owners = row_count * col_count
    experts = holding * owners
    devices = owners * tok_count
    owner = lax.axis_index("row") * col_count + lax.axis_index("col")
    assert count < 256

    normed = rms_normed(activations, norm_gain)
    gates = route_weights / jnp.sum(route_weights, axis=1, keepdims=True)
    flat_routes = routes.reshape(-1)
    target = flat_routes * CAP + rank_in_block(flat_routes, experts)
    token_ids = jnp.arange(count * chosen, dtype=jnp.int32) // chosen
    source = jnp.full((experts * CAP,), count, jnp.int32).at[target].set(token_ids)

    extra = -(-(experts * CAP) // features)
    extra = -(-extra // 8) * 8
    stride = count + extra
    table_rows = jnp.zeros((extra * features,), jnp.bfloat16)
    table_rows = table_rows.at[: experts * CAP].set(source.astype(jnp.bfloat16))
    packed = jnp.concatenate([normed, table_rows.reshape(extra, features)], axis=0)
    every = lax.all_gather(packed, ALL, axis=0, tiled=True)

    tables = every.reshape(devices, stride, features)[:, count:, :].reshape(devices, -1)
    tables = lax.dynamic_slice_in_dim(
        tables[:, : experts * CAP], owner * holding * CAP, holding * CAP, axis=1
    ).astype(jnp.int32)
    rows = tables + (jnp.arange(devices, dtype=jnp.int32) * stride)[:, None]
    rows = rows.reshape(owners, tok_count, holding, CAP).transpose(2, 1, 0, 3).reshape(-1)
    picked = jnp.take(every, rows, axis=0, mode="clip")
    picked = picked.reshape(holding, tok_count * owners * CAP, features)

    both = jnp.einsum(
        "jrd,jgfd->jrgf", picked, gate_up_weight, preferred_element_type=jnp.float32
    )
    hidden = (jax.nn.silu(both[:, :, 0, :]) * both[:, :, 1, :]).astype(jnp.bfloat16)
    partial = jnp.einsum(
        "jrf,jfd->rjd", hidden, down_weight, preferred_element_type=jnp.float32
    )
    partial = partial.astype(jnp.bfloat16).reshape(tok_count * owners, CAP, holding, features)
    summed = lax.psum_scatter(partial, "tok", scatter_dimension=0, tiled=True)

    returned = lax.all_to_all(summed, ("row", "col"), split_axis=0, concat_axis=0, tiled=True)
    expert = target // CAP
    back = (expert // holding) * (CAP * holding) + (target % CAP) * holding + expert % holding
    picked_back = jnp.take(returned.reshape(experts * CAP, features), back, axis=0)
    picked_back = picked_back.reshape(count, chosen, features)
    mixed = jnp.einsum("tk,tkd->td", gates, picked_back.astype(jnp.float32))
    return mixed.astype(jnp.bfloat16)


def solution(mesh):
    in_specs = (
        P(("row", "col", "tok"), None),
        P(),
        P(("row", "col", "tok"), None),
        P(("row", "col", "tok"), None),
        P(("row", "col"), None, "tok", None),
        P(("row", "col"), "tok", None),
    )
    out_specs = P(("row", "col", "tok"), None)
    return jax.shard_map(local, mesh=mesh, in_specs=in_specs, out_specs=out_specs, check_vma=False)
```

```python
import math

import jax
import jax.numpy as jnp
from jax import lax
from jax.sharding import PartitionSpec as P

CAP = 10
PIECES = 2


EPSILON = 1e-06

ALL = ("row", "col", "tok")


def rank_in_block(block_routes, experts):
    onehot = (block_routes[:, None] == jnp.arange(experts, dtype=jnp.int32)[None, :]).astype(
        jnp.int32
    )
    before = jnp.cumsum(onehot, axis=0) - onehot
    return jnp.sum(before * onehot, axis=1)


def rms_normed(activations, norm_gain):
    values = activations.astype(jnp.float32)
    scale = lax.rsqrt(jnp.mean(values * values, axis=-1, keepdims=True) + EPSILON)
    return (values * scale * norm_gain).astype(jnp.bfloat16)


def local(activations, norm_gain, routes, route_weights, gate_up_weight, down_weight):
    count, features = activations.shape
    chosen = routes.shape[1]
    holding = gate_up_weight.shape[0]
    row_count = lax.axis_size("row")
    col_count = lax.axis_size("col")
    tok_count = lax.axis_size("tok")
    owners = row_count * col_count
    experts = holding * owners
    devices = owners * tok_count
    owner = lax.axis_index("row") * col_count + lax.axis_index("col")
    assert count < 256

    normed = rms_normed(activations, norm_gain)
    gates = route_weights / jnp.sum(route_weights, axis=1, keepdims=True)
    flat_routes = routes.reshape(-1)
    target = flat_routes * CAP + rank_in_block(flat_routes, experts)
    token_ids = jnp.arange(count * chosen, dtype=jnp.int32) // chosen
    source = jnp.full((experts * CAP,), count, jnp.int32).at[target].set(token_ids)

    extra = -(-(experts * CAP) // features)
    extra = -(-extra // 8) * 8
    stride = count + extra
    table_rows = jnp.zeros((extra * features,), jnp.bfloat16)
    table_rows = table_rows.at[: experts * CAP].set(source.astype(jnp.bfloat16))
    packed = jnp.concatenate([normed, table_rows.reshape(extra, features)], axis=0)
    every = lax.all_gather(packed, ALL, axis=0, tiled=True)

    tables = every.reshape(devices, stride, features)[:, count:, :].reshape(devices, -1)
    tables = lax.dynamic_slice_in_dim(
        tables[:, : experts * CAP], owner * holding * CAP, holding * CAP, axis=1
    ).astype(jnp.int32)
    rows = tables + (jnp.arange(devices, dtype=jnp.int32) * stride)[:, None]
    rows = rows.reshape(owners, tok_count, holding, CAP).transpose(2, 1, 0, 3).reshape(-1)
    rows = rows.reshape(holding, -1)
    pieces = math.gcd(holding, PIECES)
    width = holding // pieces
    returned = []
    sums = []
    for piece in range(pieces):
        span = slice(piece * width, (piece + 1) * width)
        picked = jnp.take(every, rows[span].reshape(-1), axis=0, mode="clip")
        picked = picked.reshape(width, tok_count * owners * CAP, features)
        both = jnp.einsum(
            "jrd,jgfd->jrgf", picked, gate_up_weight[span], preferred_element_type=jnp.float32
        )
        hidden = (jax.nn.silu(both[:, :, 0, :]) * both[:, :, 1, :]).astype(jnp.bfloat16)
        partial = jnp.einsum(
            "jrf,jfd->jrd", hidden, down_weight[span], preferred_element_type=jnp.float32
        )
        partial = partial.astype(jnp.bfloat16).reshape(width, tok_count * owners, CAP, features)
        partial = partial.transpose(1, 2, 0, 3).reshape(tok_count * owners, CAP * width, features)
        if sums:
            partial, _ = lax.optimization_barrier((partial, sums[-1]))
        sums.append(lax.psum_scatter(partial, "tok", scatter_dimension=0, tiled=True))
        returned.append(
            lax.all_to_all(sums[-1], ("row", "col"), split_axis=0, concat_axis=0, tiled=True)
        )
    returned = jnp.concatenate(returned, axis=1)
    expert = target // CAP
    back = (
        (expert // width) * (CAP * width) + (target % CAP) * width + expert % width
    )
    picked_back = jnp.take(returned.reshape(experts * CAP, features), back, axis=0)
    picked_back = picked_back.reshape(count, chosen, features)
    mixed = jnp.einsum("tk,tkd->td", gates, picked_back.astype(jnp.float32))
    return mixed.astype(jnp.bfloat16)


def solution(mesh):
    in_specs = (
        P(("row", "col", "tok"), None),
        P(),
        P(("row", "col", "tok"), None),
        P(("row", "col", "tok"), None),
        P(("row", "col"), None, "tok", None),
        P(("row", "col"), "tok", None),
    )
    out_specs = P(("row", "col", "tok"), None)
    return jax.shard_map(local, mesh=mesh, in_specs=in_specs, out_specs=out_specs, check_vma=False)
```

```python
import math

import jax
import jax.numpy as jnp
from jax import lax
from jax.sharding import PartitionSpec as P

CAP = 10
PIECES = 2


EPSILON = 1e-06

ALL = ("row", "col", "tok")


def rank_in_block(block_routes, experts):
    onehot = (block_routes[:, None] == jnp.arange(experts, dtype=jnp.int32)[None, :]).astype(
        jnp.int32
    )
    before = jnp.cumsum(onehot, axis=0) - onehot
    return jnp.sum(before * onehot, axis=1)


def rms_normed(activations, norm_gain):
    values = activations.astype(jnp.float32)
    scale = lax.rsqrt(jnp.mean(values * values, axis=-1, keepdims=True) + EPSILON)
    return (values * scale * norm_gain).astype(jnp.bfloat16)


def local(activations, norm_gain, routes, route_weights, gate_up_weight, down_weight):
    count, features = activations.shape
    chosen = routes.shape[1]
    holding = gate_up_weight.shape[0]
    row_count = lax.axis_size("row")
    col_count = lax.axis_size("col")
    tok_count = lax.axis_size("tok")
    owners = row_count * col_count
    experts = holding * owners
    devices = owners * tok_count
    owner = lax.axis_index("row") * col_count + lax.axis_index("col")
    assert count < 256

    normed = rms_normed(activations, norm_gain)
    gates = route_weights / jnp.sum(route_weights, axis=1, keepdims=True)
    flat_routes = routes.reshape(-1)
    target = flat_routes * CAP + rank_in_block(flat_routes, experts)
    token_ids = jnp.arange(count * chosen, dtype=jnp.int32) // chosen
    source = jnp.full((experts * CAP,), count, jnp.int32).at[target].set(token_ids)

    extra = -(-(experts * CAP) // features)
    extra = -(-extra // 8) * 8
    stride = count + extra
    table_rows = jnp.zeros((extra * features,), jnp.bfloat16)
    table_rows = table_rows.at[: experts * CAP].set(source.astype(jnp.bfloat16))
    lanes = features // 128
    packed = jnp.concatenate([normed, table_rows.reshape(extra, features)], axis=0)
    every = lax.all_gather(packed.reshape(stride, lanes, 128), ALL, axis=0, tiled=True)

    tables = every.reshape(devices, stride, lanes, 128)[:, count:].reshape(devices, -1)
    tables = lax.dynamic_slice_in_dim(
        tables[:, : experts * CAP], owner * holding * CAP, holding * CAP, axis=1
    ).astype(jnp.int32)
    rows = tables + (jnp.arange(devices, dtype=jnp.int32) * stride)[:, None]
    rows = rows.reshape(owners, tok_count, holding, CAP).transpose(2, 1, 0, 3).reshape(-1)
    rows = rows.reshape(holding, -1)
    pieces = math.gcd(holding, PIECES)
    width = holding // pieces
    returned = []
    sums = []
    for piece in range(pieces):
        span = slice(piece * width, (piece + 1) * width)
        picked = jnp.take(every, rows[span].reshape(-1), axis=0, mode="clip")
        picked = picked.reshape(width, tok_count * owners * CAP, features)
        both = jnp.einsum(
            "jrd,jgfd->jrgf", picked, gate_up_weight[span], preferred_element_type=jnp.float32
        )
        hidden = (jax.nn.silu(both[:, :, 0, :]) * both[:, :, 1, :]).astype(jnp.bfloat16)
        partial = jnp.einsum(
            "jrf,jfd->jrd", hidden, down_weight[span], preferred_element_type=jnp.float32
        )
        partial = partial.astype(jnp.bfloat16).reshape(width, tok_count * owners, CAP, features)
        partial = partial.transpose(1, 2, 0, 3).reshape(tok_count * owners, CAP * width, features)
        if sums:
            partial, _ = lax.optimization_barrier((partial, sums[-1]))
        sums.append(lax.psum_scatter(partial, "tok", scatter_dimension=0, tiled=True))
        returned.append(
            lax.all_to_all(sums[-1], ("row", "col"), split_axis=0, concat_axis=0, tiled=True)
        )
    returned = jnp.concatenate(returned, axis=1)
    expert = target // CAP
    back = (
        (expert // width) * (CAP * width) + (target % CAP) * width + expert % width
    )
    picked_back = jnp.take(returned.reshape(experts * CAP, features), back, axis=0)
    picked_back = picked_back.reshape(count, chosen, features)
    mixed = jnp.einsum("tk,tkd->td", gates, picked_back.astype(jnp.float32))
    return mixed.astype(jnp.bfloat16)


def solution(mesh):
    in_specs = (
        P(("row", "col", "tok"), None),
        P(),
        P(("row", "col", "tok"), None),
        P(("row", "col", "tok"), None),
        P(("row", "col"), None, "tok", None),
        P(("row", "col"), "tok", None),
    )
    out_specs = P(("row", "col", "tok"), None)
    return jax.shard_map(local, mesh=mesh, in_specs=in_specs, out_specs=out_specs, check_vma=False)
```

```python
import math

import jax
import jax.numpy as jnp
from jax import lax
from jax.sharding import PartitionSpec as P

CAP = 10
PIECES = 2


EPSILON = 1e-06

ALL = ("row", "col", "tok")


def rank_in_block(block_routes, experts):
    onehot = (block_routes[:, None] == jnp.arange(experts, dtype=jnp.int32)[None, :]).astype(
        jnp.int32
    )
    before = jnp.cumsum(onehot, axis=0) - onehot
    return jnp.sum(before * onehot, axis=1)


def rms_normed(activations, norm_gain):
    values = activations.astype(jnp.float32)
    scale = lax.rsqrt(jnp.mean(values * values, axis=-1, keepdims=True) + EPSILON)
    return (values * scale * norm_gain).astype(jnp.bfloat16)


def reduce_over_tok(partial, tok_count):
    if tok_count % 2:
        return lax.psum_scatter(partial, "tok", scatter_dimension=0, tiled=True)
    halves = tok_count // 2
    t = lax.axis_index("tok")
    core = t % 2
    upper = t // 2
    blocks = partial.reshape(halves, 2, -1, *partial.shape[2:])
    kept = lax.dynamic_index_in_dim(blocks, core, axis=1, keepdims=False)
    sent = lax.dynamic_index_in_dim(blocks, 1 - core, axis=1, keepdims=False)
    swap_core = [(i, i ^ 1) for i in range(tok_count)]
    got = lax.ppermute(sent, "tok", swap_core)
    pairs = kept.astype(jnp.float32) + got.astype(jnp.float32)
    if halves == 1:
        return pairs[0]
    if halves != 2:
        pairs = pairs.astype(jnp.bfloat16)
        return lax.psum_scatter(pairs, "tok", scatter_dimension=0, tiled=True)
    kept = lax.dynamic_index_in_dim(pairs, upper, axis=0, keepdims=False)
    sent = lax.dynamic_index_in_dim(pairs, 1 - upper, axis=0, keepdims=False)
    swap_upper = [(i, i ^ 2) for i in range(tok_count)]
    got = lax.ppermute(sent.astype(jnp.bfloat16), "tok", swap_upper)
    return (kept + got.astype(jnp.float32)).astype(jnp.bfloat16)


def local(activations, norm_gain, routes, route_weights, gate_up_weight, down_weight):
    count, features = activations.shape
    chosen = routes.shape[1]
    holding = gate_up_weight.shape[0]
    row_count = lax.axis_size("row")
    col_count = lax.axis_size("col")
    tok_count = lax.axis_size("tok")
    owners = row_count * col_count
    experts = holding * owners
    devices = owners * tok_count
    owner = lax.axis_index("row") * col_count + lax.axis_index("col")
    assert count < 256

    normed = rms_normed(activations, norm_gain)
    gates = route_weights / jnp.sum(route_weights, axis=1, keepdims=True)
    flat_routes = routes.reshape(-1)
    target = flat_routes * CAP + rank_in_block(flat_routes, experts)
    token_ids = jnp.arange(count * chosen, dtype=jnp.int32) // chosen
    source = jnp.full((experts * CAP,), count, jnp.int32).at[target].set(token_ids)

    extra = -(-(experts * CAP) // features)
    extra = -(-extra // 8) * 8
    stride = count + extra
    table_rows = jnp.zeros((extra * features,), jnp.bfloat16)
    table_rows = table_rows.at[: experts * CAP].set(source.astype(jnp.bfloat16))
    packed = jnp.concatenate([normed, table_rows.reshape(extra, features)], axis=0)
    every = lax.all_gather(packed, ALL, axis=0, tiled=True)

    tables = every.reshape(devices, stride, features)[:, count:, :].reshape(devices, -1)
    tables = lax.dynamic_slice_in_dim(
        tables[:, : experts * CAP], owner * holding * CAP, holding * CAP, axis=1
    ).astype(jnp.int32)
    rows = tables + (jnp.arange(devices, dtype=jnp.int32) * stride)[:, None]
    rows = rows.reshape(owners, tok_count, holding, CAP).transpose(2, 1, 0, 3).reshape(-1)
    rows = rows.reshape(holding, -1)
    pieces = math.gcd(holding, PIECES)
    width = holding // pieces
    returned = []
    sums = []
    for piece in range(pieces):
        span = slice(piece * width, (piece + 1) * width)
        picked = jnp.take(every, rows[span].reshape(-1), axis=0, mode="clip")
        picked = picked.reshape(width, tok_count * owners * CAP, features)
        both = jnp.einsum(
            "jrd,jgfd->jrgf", picked, gate_up_weight[span], preferred_element_type=jnp.float32
        )
        hidden = (jax.nn.silu(both[:, :, 0, :]) * both[:, :, 1, :]).astype(jnp.bfloat16)
        partial = jnp.einsum(
            "jrf,jfd->jrd", hidden, down_weight[span], preferred_element_type=jnp.float32
        )
        partial = partial.astype(jnp.bfloat16).reshape(width, tok_count * owners, CAP, features)
        partial = partial.transpose(1, 2, 0, 3).reshape(tok_count * owners, CAP * width, features)
        sums.append(reduce_over_tok(partial, tok_count).reshape(owners, CAP * width, features))
        returned.append(
            lax.all_to_all(sums[-1], ("row", "col"), split_axis=0, concat_axis=0, tiled=True)
        )
    returned = jnp.concatenate(returned, axis=1)
    expert = target // CAP
    back = (
        (expert // width) * (CAP * width) + (target % CAP) * width + expert % width
    )
    picked_back = jnp.take(returned.reshape(experts * CAP, features), back, axis=0)
    picked_back = picked_back.reshape(count, chosen, features)
    mixed = jnp.einsum("tk,tkd->td", gates, picked_back.astype(jnp.float32))
    return mixed.astype(jnp.bfloat16)


def solution(mesh):
    in_specs = (
        P(("row", "col", "tok"), None),
        P(),
        P(("row", "col", "tok"), None),
        P(("row", "col", "tok"), None),
        P(("row", "col"), None, "tok", None),
        P(("row", "col"), "tok", None),
    )
    out_specs = P(("row", "col", "tok"), None)
    return jax.shard_map(local, mesh=mesh, in_specs=in_specs, out_specs=out_specs, check_vma=False)
```

```python
import math

import jax
import jax.numpy as jnp
from jax import lax
from jax.sharding import PartitionSpec as P

CAP = 10
PIECES = 2


EPSILON = 1e-06

ALL = ("row", "col", "tok")


def rank_in_block(block_routes, experts):
    onehot = (block_routes[:, None] == jnp.arange(experts, dtype=jnp.int32)[None, :]).astype(
        jnp.int32
    )
    before = jnp.cumsum(onehot, axis=0) - onehot
    return jnp.sum(before * onehot, axis=1)


def rms_normed(activations, norm_gain):
    values = activations.astype(jnp.float32)
    scale = lax.rsqrt(jnp.mean(values * values, axis=-1, keepdims=True) + EPSILON)
    return (values * scale * norm_gain).astype(jnp.bfloat16)


def local(activations, norm_gain, routes, route_weights, gate_up_weight, down_weight):
    count, features = activations.shape
    chosen = routes.shape[1]
    holding = gate_up_weight.shape[0]
    row_count = lax.axis_size("row")
    col_count = lax.axis_size("col")
    tok_count = lax.axis_size("tok")
    owners = row_count * col_count
    experts = holding * owners
    devices = owners * tok_count
    owner = lax.axis_index("row") * col_count + lax.axis_index("col")
    assert count < 256

    normed = rms_normed(activations, norm_gain)
    gates = route_weights / jnp.sum(route_weights, axis=1, keepdims=True)
    flat_routes = routes.reshape(-1)
    target = flat_routes * CAP + rank_in_block(flat_routes, experts)
    token_ids = jnp.arange(count * chosen, dtype=jnp.int32) // chosen
    source = jnp.full((experts * CAP,), count, jnp.int32).at[target].set(token_ids)

    extra = -(-(experts * CAP) // features)
    extra = -(-extra // 8) * 8
    stride = count + extra
    table_rows = jnp.zeros((extra * features,), jnp.bfloat16)
    table_rows = table_rows.at[: experts * CAP].set(source.astype(jnp.bfloat16))
    packed = jnp.concatenate([normed, table_rows.reshape(extra, features)], axis=0)
    every = lax.all_gather(packed, ALL, axis=0, tiled=True)

    tables = every.reshape(devices, stride, features)[:, count:, :].reshape(devices, -1)
    tables = lax.dynamic_slice_in_dim(
        tables[:, : experts * CAP], owner * holding * CAP, holding * CAP, axis=1
    ).astype(jnp.int32)
    rows = tables + (jnp.arange(devices, dtype=jnp.int32) * stride)[:, None]
    rows = rows.reshape(owners, tok_count, holding, CAP).transpose(2, 1, 0, 3).reshape(-1)
    rows = rows.reshape(holding, -1)
    pieces = math.gcd(holding, PIECES)
    width = holding // pieces
    returned = []
    sums = []
    for piece in range(pieces):
        span = slice(piece * width, (piece + 1) * width)
        picked = jnp.take(every, rows[span].reshape(-1), axis=0, mode="clip")
        picked = picked.reshape(width, tok_count * owners * CAP, features)
        both = jnp.einsum(
            "jrd,jgfd->jrgf", picked, gate_up_weight[span], preferred_element_type=jnp.float32
        )
        hidden = (jax.nn.silu(both[:, :, 0, :]) * both[:, :, 1, :]).astype(jnp.bfloat16)
        partial = jnp.einsum(
            "jrf,jfd->jrd", hidden, down_weight[span], preferred_element_type=jnp.float32
        )
        partial = partial.astype(jnp.bfloat16)
        if sums:
            partial, _ = lax.optimization_barrier((partial, sums[-1]))
        sums.append(lax.psum_scatter(partial, "tok", scatter_dimension=1, tiled=True))
        summed = sums[-1].reshape(width, owners, CAP, features).transpose(1, 0, 2, 3)
        summed = summed.reshape(owners, width * CAP, features)
        returned.append(
            lax.all_to_all(summed, ("row", "col"), split_axis=0, concat_axis=0, tiled=True)
        )
    returned = jnp.concatenate(returned, axis=1)
    picked_back = jnp.take(returned.reshape(experts * CAP, features), target, axis=0)
    picked_back = picked_back.reshape(count, chosen, features)
    mixed = jnp.einsum("tk,tkd->td", gates, picked_back.astype(jnp.float32))
    return mixed.astype(jnp.bfloat16)


def solution(mesh):
    in_specs = (
        P(("row", "col", "tok"), None),
        P(),
        P(("row", "col", "tok"), None),
        P(("row", "col", "tok"), None),
        P(("row", "col"), None, "tok", None),
        P(("row", "col"), "tok", None),
    )
    out_specs = P(("row", "col", "tok"), None)
    return jax.shard_map(local, mesh=mesh, in_specs=in_specs, out_specs=out_specs, check_vma=False)
```

```python
import math

import jax
import jax.numpy as jnp
from jax import lax
from jax.sharding import PartitionSpec as P

CAP = 10
PIECES = 4


EPSILON = 1e-06

ALL = ("row", "col", "tok")


def rank_in_block(block_routes, experts):
    onehot = (block_routes[:, None] == jnp.arange(experts, dtype=jnp.int32)[None, :]).astype(
        jnp.int32
    )
    before = jnp.cumsum(onehot, axis=0) - onehot
    return jnp.sum(before * onehot, axis=1)


def rms_normed(activations, norm_gain):
    values = activations.astype(jnp.float32)
    scale = lax.rsqrt(jnp.mean(values * values, axis=-1, keepdims=True) + EPSILON)
    return (values * scale * norm_gain).astype(jnp.bfloat16)


def local(activations, norm_gain, routes, route_weights, gate_up_weight, down_weight):
    count, features = activations.shape
    chosen = routes.shape[1]
    holding = gate_up_weight.shape[0]
    row_count = lax.axis_size("row")
    col_count = lax.axis_size("col")
    tok_count = lax.axis_size("tok")
    owners = row_count * col_count
    experts = holding * owners
    devices = owners * tok_count
    owner = lax.axis_index("row") * col_count + lax.axis_index("col")
    assert count < 256

    normed = rms_normed(activations, norm_gain)
    gates = route_weights / jnp.sum(route_weights, axis=1, keepdims=True)
    flat_routes = routes.reshape(-1)
    target = flat_routes * CAP + rank_in_block(flat_routes, experts)
    token_ids = jnp.arange(count * chosen, dtype=jnp.int32) // chosen
    source = jnp.full((experts * CAP,), count, jnp.int32).at[target].set(token_ids)

    extra = -(-(experts * CAP) // features)
    extra = -(-extra // 8) * 8
    stride = count + extra
    table_rows = jnp.zeros((extra * features,), jnp.bfloat16)
    table_rows = table_rows.at[: experts * CAP].set(source.astype(jnp.bfloat16))
    packed = jnp.concatenate([normed, table_rows.reshape(extra, features)], axis=0)
    every = lax.all_gather(packed, ALL, axis=0, tiled=True)

    tables = every.reshape(devices, stride, features)[:, count:, :].reshape(devices, -1)
    tables = lax.dynamic_slice_in_dim(
        tables[:, : experts * CAP], owner * holding * CAP, holding * CAP, axis=1
    ).astype(jnp.int32)
    rows = tables + (jnp.arange(devices, dtype=jnp.int32) * stride)[:, None]
    rows = rows.reshape(owners, tok_count, holding, CAP).transpose(2, 1, 0, 3).reshape(-1)
    rows = rows.reshape(holding, -1)
    pieces = math.gcd(holding, PIECES)
    width = holding // pieces
    returned = []
    sums = []
    for piece in range(pieces):
        span = slice(piece * width, (piece + 1) * width)
        picked = jnp.take(every, rows[span].reshape(-1), axis=0, mode="clip")
        picked = picked.reshape(width, tok_count * owners * CAP, features)
        both = jnp.einsum(
            "jrd,jgfd->jrgf", picked, gate_up_weight[span], preferred_element_type=jnp.float32
        )
        hidden = (jax.nn.silu(both[:, :, 0, :]) * both[:, :, 1, :]).astype(jnp.bfloat16)
        partial = jnp.einsum(
            "jrf,jfd->jrd", hidden, down_weight[span], preferred_element_type=jnp.float32
        )
        partial = partial.astype(jnp.bfloat16)
        if sums:
            partial, _ = lax.optimization_barrier((partial, sums[-1]))
        sums.append(lax.psum_scatter(partial, "tok", scatter_dimension=1, tiled=True))
        summed = sums[-1].reshape(width, owners, CAP, features).transpose(1, 0, 2, 3)
        summed = summed.reshape(owners, width * CAP, features)
        returned.append(
            lax.all_to_all(summed, ("row", "col"), split_axis=0, concat_axis=0, tiled=True)
        )
    returned = jnp.concatenate(returned, axis=1)
    picked_back = jnp.take(returned.reshape(experts * CAP, features), target, axis=0)
    picked_back = picked_back.reshape(count, chosen, features)
    mixed = jnp.einsum("tk,tkd->td", gates, picked_back.astype(jnp.float32))
    return mixed.astype(jnp.bfloat16)


def solution(mesh):
    in_specs = (
        P(("row", "col", "tok"), None),
        P(),
        P(("row", "col", "tok"), None),
        P(("row", "col", "tok"), None),
        P(("row", "col"), None, "tok", None),
        P(("row", "col"), "tok", None),
    )
    out_specs = P(("row", "col", "tok"), None)
    return jax.shard_map(local, mesh=mesh, in_specs=in_specs, out_specs=out_specs, check_vma=False)
```

```python
import math

import jax
import jax.numpy as jnp
from jax import lax
from jax.sharding import PartitionSpec as P

CAP = 10
PIECES = 4


EPSILON = 1e-06

ALL = ("row", "col", "tok")


def rank_in_block(block_routes, experts):
    onehot = (block_routes[:, None] == jnp.arange(experts, dtype=jnp.int32)[None, :]).astype(
        jnp.int32
    )
    before = jnp.cumsum(onehot, axis=0) - onehot
    return jnp.sum(before * onehot, axis=1)


def rms_normed(activations, norm_gain):
    values = activations.astype(jnp.float32)
    scale = lax.rsqrt(jnp.mean(values * values, axis=-1, keepdims=True) + EPSILON)
    return (values * scale * norm_gain).astype(jnp.bfloat16)


def local(activations, norm_gain, routes, route_weights, gate_up_weight, down_weight):
    count, features = activations.shape
    chosen = routes.shape[1]
    holding = gate_up_weight.shape[0]
    row_count = lax.axis_size("row")
    col_count = lax.axis_size("col")
    tok_count = lax.axis_size("tok")
    owners = row_count * col_count
    experts = holding * owners
    devices = owners * tok_count
    owner = lax.axis_index("row") * col_count + lax.axis_index("col")
    assert count < 256

    normed = rms_normed(activations, norm_gain)
    gates = route_weights / jnp.sum(route_weights, axis=1, keepdims=True)
    flat_routes = routes.reshape(-1)
    target = flat_routes * CAP + rank_in_block(flat_routes, experts)
    token_ids = jnp.arange(count * chosen, dtype=jnp.int32) // chosen
    source = jnp.full((experts * CAP,), count, jnp.int32).at[target].set(token_ids)

    extra = -(-(experts * CAP) // features)
    extra = -(-extra // 8) * 8
    stride = count + extra
    table_rows = jnp.zeros((extra * features,), jnp.bfloat16)
    table_rows = table_rows.at[: experts * CAP].set(source.astype(jnp.bfloat16))
    packed = jnp.concatenate([normed, table_rows.reshape(extra, features)], axis=0)
    every = lax.all_gather(packed, ALL, axis=0, tiled=True)

    tables = every.reshape(devices, stride, features)[:, count:, :].reshape(devices, -1)
    tables = lax.dynamic_slice_in_dim(
        tables[:, : experts * CAP], owner * holding * CAP, holding * CAP, axis=1
    ).astype(jnp.int32)
    rows = tables + (jnp.arange(devices, dtype=jnp.int32) * stride)[:, None]
    rows = rows.reshape(owners, tok_count, holding, CAP).transpose(2, 1, 0, 3).reshape(-1)
    rows = rows.reshape(holding, -1)
    pieces = math.gcd(holding, PIECES)
    width = holding // pieces
    returned = []
    sums = []
    for piece in range(pieces):
        span = slice(piece * width, (piece + 1) * width)
        picked = jnp.take(every, rows[span].reshape(-1), axis=0, mode="clip")
        picked = picked.reshape(width, tok_count * owners * CAP, features)
        both = jnp.einsum(
            "jrd,jgfd->jrgf", picked, gate_up_weight[span], preferred_element_type=jnp.float32
        )
        hidden = (jax.nn.silu(both[:, :, 0, :]) * both[:, :, 1, :]).astype(jnp.bfloat16)
        partial = jnp.einsum(
            "jrf,jfd->jrd", hidden, down_weight[span], preferred_element_type=jnp.float32
        )
        partial = partial.astype(jnp.bfloat16)
        if sums:
            partial, _ = lax.optimization_barrier((partial, (sums[-1], returned[:-1])))
        sums.append(lax.psum_scatter(partial, "tok", scatter_dimension=1, tiled=True))
        summed = sums[-1].reshape(width, owners, CAP, features).transpose(1, 0, 2, 3)
        summed = summed.reshape(owners, width * CAP, features)
        returned.append(
            lax.all_to_all(summed, ("row", "col"), split_axis=0, concat_axis=0, tiled=True)
        )
    returned = jnp.concatenate(returned, axis=1)
    picked_back = jnp.take(returned.reshape(experts * CAP, features), target, axis=0)
    picked_back = picked_back.reshape(count, chosen, features)
    mixed = jnp.einsum("tk,tkd->td", gates, picked_back.astype(jnp.float32))
    return mixed.astype(jnp.bfloat16)


def solution(mesh):
    in_specs = (
        P(("row", "col", "tok"), None),
        P(),
        P(("row", "col", "tok"), None),
        P(("row", "col", "tok"), None),
        P(("row", "col"), None, "tok", None),
        P(("row", "col"), "tok", None),
    )
    out_specs = P(("row", "col", "tok"), None)
    return jax.shard_map(local, mesh=mesh, in_specs=in_specs, out_specs=out_specs, check_vma=False)
```

```python
import math

import jax
import jax.numpy as jnp
from jax import lax
from jax.sharding import PartitionSpec as P

CAP = 10
PIECES = 4


EPSILON = 1e-06

ALL = ("row", "col", "tok")


def rank_in_block(block_routes, experts):
    onehot = (block_routes[:, None] == jnp.arange(experts, dtype=jnp.int32)[None, :]).astype(
        jnp.int32
    )
    before = jnp.cumsum(onehot, axis=0) - onehot
    return jnp.sum(before * onehot, axis=1)


def rms_normed(activations, norm_gain):
    values = activations.astype(jnp.float32)
    scale = lax.rsqrt(jnp.mean(values * values, axis=-1, keepdims=True) + EPSILON)
    return (values * scale * norm_gain).astype(jnp.bfloat16)


def local(activations, norm_gain, routes, route_weights, gate_up_weight, down_weight):
    count, features = activations.shape
    chosen = routes.shape[1]
    holding = gate_up_weight.shape[0]
    row_count = lax.axis_size("row")
    col_count = lax.axis_size("col")
    tok_count = lax.axis_size("tok")
    owners = row_count * col_count
    experts = holding * owners
    devices = owners * tok_count
    owner = lax.axis_index("row") * col_count + lax.axis_index("col")
    assert count < 256

    normed = rms_normed(activations, norm_gain)
    gates = route_weights / jnp.sum(route_weights, axis=1, keepdims=True)
    flat_routes = routes.reshape(-1)
    target = flat_routes * CAP + rank_in_block(flat_routes, experts)
    token_ids = jnp.arange(count * chosen, dtype=jnp.int32) // chosen
    source = jnp.full((experts * CAP,), count, jnp.int32).at[target].set(token_ids)

    extra = -(-(experts * CAP) // features)
    extra = -(-extra // 8) * 8
    stride = count + extra
    table_rows = jnp.zeros((extra * features,), jnp.bfloat16)
    table_rows = table_rows.at[: experts * CAP].set(source.astype(jnp.bfloat16))
    packed = jnp.concatenate([normed, table_rows.reshape(extra, features)], axis=0)
    every = lax.all_gather(packed, "tok", axis=0, tiled=True)
    every = lax.all_gather(every, ("row", "col"), axis=0, tiled=True)

    tables = every.reshape(devices, stride, features)[:, count:, :].reshape(devices, -1)
    tables = lax.dynamic_slice_in_dim(
        tables[:, : experts * CAP], owner * holding * CAP, holding * CAP, axis=1
    ).astype(jnp.int32)
    rows = tables + (jnp.arange(devices, dtype=jnp.int32) * stride)[:, None]
    rows = rows.reshape(owners, tok_count, holding, CAP).transpose(2, 1, 0, 3).reshape(-1)
    rows = rows.reshape(holding, -1)
    pieces = math.gcd(holding, PIECES)
    width = holding // pieces
    returned = []
    sums = []
    for piece in range(pieces):
        span = slice(piece * width, (piece + 1) * width)
        picked = jnp.take(every, rows[span].reshape(-1), axis=0, mode="clip")
        picked = picked.reshape(width, tok_count * owners * CAP, features)
        both = jnp.einsum(
            "jrd,jgfd->jrgf", picked, gate_up_weight[span], preferred_element_type=jnp.float32
        )
        hidden = (jax.nn.silu(both[:, :, 0, :]) * both[:, :, 1, :]).astype(jnp.bfloat16)
        partial = jnp.einsum(
            "jrf,jfd->jrd", hidden, down_weight[span], preferred_element_type=jnp.float32
        )
        partial = partial.astype(jnp.bfloat16)
        if sums:
            partial, _ = lax.optimization_barrier((partial, (sums[-1], returned[:-1])))
        sums.append(lax.psum_scatter(partial, "tok", scatter_dimension=1, tiled=True))
        summed = sums[-1].reshape(width, owners, CAP, features).transpose(1, 0, 2, 3)
        summed = summed.reshape(owners, width * CAP, features)
        returned.append(
            lax.all_to_all(summed, ("row", "col"), split_axis=0, concat_axis=0, tiled=True)
        )
    returned = jnp.concatenate(returned, axis=1)
    picked_back = jnp.take(returned.reshape(experts * CAP, features), target, axis=0)
    picked_back = picked_back.reshape(count, chosen, features)
    mixed = jnp.einsum("tk,tkd->td", gates, picked_back.astype(jnp.float32))
    return mixed.astype(jnp.bfloat16)


def solution(mesh):
    in_specs = (
        P(("row", "col", "tok"), None),
        P(),
        P(("row", "col", "tok"), None),
        P(("row", "col", "tok"), None),
        P(("row", "col"), None, "tok", None),
        P(("row", "col"), "tok", None),
    )
    out_specs = P(("row", "col", "tok"), None)
    return jax.shard_map(local, mesh=mesh, in_specs=in_specs, out_specs=out_specs, check_vma=False)
```

```python
import math

import jax
import jax.numpy as jnp
from jax import lax
from jax.sharding import PartitionSpec as P

CAP = 10
PIECES = 4


EPSILON = 1e-06

ALL = ("row", "col", "tok")


def rank_in_block(block_routes, experts):
    onehot = (block_routes[:, None] == jnp.arange(experts, dtype=jnp.int32)[None, :]).astype(
        jnp.int32
    )
    before = jnp.cumsum(onehot, axis=0) - onehot
    return jnp.sum(before * onehot, axis=1)


def rms_normed(activations, norm_gain):
    values = activations.astype(jnp.float32)
    scale = lax.rsqrt(jnp.mean(values * values, axis=-1, keepdims=True) + EPSILON)
    return (values * scale * norm_gain).astype(jnp.bfloat16)


def local(activations, norm_gain, routes, route_weights, gate_up_weight, down_weight):
    count, features = activations.shape
    chosen = routes.shape[1]
    holding = gate_up_weight.shape[0]
    row_count = lax.axis_size("row")
    col_count = lax.axis_size("col")
    tok_count = lax.axis_size("tok")
    owners = row_count * col_count
    experts = holding * owners
    devices = owners * tok_count
    owner = lax.axis_index("row") * col_count + lax.axis_index("col")
    assert count < 256

    normed = rms_normed(activations, norm_gain)
    gates = route_weights / jnp.sum(route_weights, axis=1, keepdims=True)
    flat_routes = routes.reshape(-1)
    target = flat_routes * CAP + rank_in_block(flat_routes, experts)
    token_ids = jnp.arange(count * chosen, dtype=jnp.int32) // chosen
    source = jnp.full((experts * CAP,), count, jnp.int32).at[target].set(token_ids)

    half = features // 2
    extra = -(-(experts * CAP) // half)
    extra = -(-extra // 8) * 8
    stride = count + extra
    table_rows = jnp.zeros((extra * half,), jnp.bfloat16)
    table_rows = table_rows.at[: experts * CAP].set(source.astype(jnp.bfloat16))
    packed = jnp.concatenate([normed[:, :half], table_rows.reshape(extra, half)], axis=0)
    every = lax.all_gather(packed, ALL, axis=0, tiled=True)
    later = jnp.concatenate([normed[:, half:], jnp.zeros((extra, half), jnp.bfloat16)], axis=0)
    later, _ = lax.optimization_barrier((later, every))
    every_later = lax.all_gather(later, ALL, axis=0, tiled=True)

    tables = every.reshape(devices, stride, half)[:, count:, :].reshape(devices, -1)
    tables = lax.dynamic_slice_in_dim(
        tables[:, : experts * CAP], owner * holding * CAP, holding * CAP, axis=1
    ).astype(jnp.int32)
    rows = tables + (jnp.arange(devices, dtype=jnp.int32) * stride)[:, None]
    rows = rows.reshape(owners, tok_count, holding, CAP).transpose(2, 1, 0, 3).reshape(-1)
    rows = rows.reshape(holding, -1)
    pieces = math.gcd(holding, PIECES)
    width = holding // pieces
    returned = []
    sums = []
    for piece in range(pieces):
        span = slice(piece * width, (piece + 1) * width)
        both = 0
        for part, gathered in ((slice(0, half), every), (slice(half, features), every_later)):
            picked = jnp.take(gathered, rows[span].reshape(-1), axis=0, mode="clip")
            picked = picked.reshape(width, tok_count * owners * CAP, half)
            both = both + jnp.einsum(
                "jrd,jgfd->jrgf",
                picked,
                gate_up_weight[span][..., part],
                preferred_element_type=jnp.float32,
            )
        hidden = (jax.nn.silu(both[:, :, 0, :]) * both[:, :, 1, :]).astype(jnp.bfloat16)
        partial = jnp.einsum(
            "jrf,jfd->jrd", hidden, down_weight[span], preferred_element_type=jnp.float32
        )
        partial = partial.astype(jnp.bfloat16)
        if sums:
            partial, _ = lax.optimization_barrier((partial, (sums[-1], returned[:-1])))
        sums.append(lax.psum_scatter(partial, "tok", scatter_dimension=1, tiled=True))
        summed = sums[-1].reshape(width, owners, CAP, features).transpose(1, 0, 2, 3)
        summed = summed.reshape(owners, width * CAP, features)
        returned.append(
            lax.all_to_all(summed, ("row", "col"), split_axis=0, concat_axis=0, tiled=True)
        )
    returned = jnp.concatenate(returned, axis=1)
    picked_back = jnp.take(returned.reshape(experts * CAP, features), target, axis=0)
    picked_back = picked_back.reshape(count, chosen, features)
    mixed = jnp.einsum("tk,tkd->td", gates, picked_back.astype(jnp.float32))
    return mixed.astype(jnp.bfloat16)


def solution(mesh):
    in_specs = (
        P(("row", "col", "tok"), None),
        P(),
        P(("row", "col", "tok"), None),
        P(("row", "col", "tok"), None),
        P(("row", "col"), None, "tok", None),
        P(("row", "col"), "tok", None),
    )
    out_specs = P(("row", "col", "tok"), None)
    return jax.shard_map(local, mesh=mesh, in_specs=in_specs, out_specs=out_specs, check_vma=False)
```

```python
import math

import jax
import jax.numpy as jnp
from jax import lax
from jax.sharding import PartitionSpec as P

CAP = 10
PIECES = 4


EPSILON = 1e-06

ALL = ("row", "col", "tok")


def rank_in_block(block_routes, experts):
    onehot = (block_routes[:, None] == jnp.arange(experts, dtype=jnp.int32)[None, :]).astype(
        jnp.int32
    )
    before = jnp.cumsum(onehot, axis=0) - onehot
    return jnp.sum(before * onehot, axis=1)


def rms_normed(activations, norm_gain):
    values = activations.astype(jnp.float32)
    scale = lax.rsqrt(jnp.mean(values * values, axis=-1, keepdims=True) + EPSILON)
    return (values * scale * norm_gain).astype(jnp.bfloat16)


def local(activations, norm_gain, routes, route_weights, gate_up_weight, down_weight):
    count, features = activations.shape
    chosen = routes.shape[1]
    holding = gate_up_weight.shape[0]
    row_count = lax.axis_size("row")
    col_count = lax.axis_size("col")
    tok_count = lax.axis_size("tok")
    owners = row_count * col_count
    experts = holding * owners
    devices = owners * tok_count
    owner = lax.axis_index("row") * col_count + lax.axis_index("col")
    assert count < 256

    normed = rms_normed(activations, norm_gain)
    gates = route_weights / jnp.sum(route_weights, axis=1, keepdims=True)
    flat_routes = routes.reshape(-1)
    target = flat_routes * CAP + rank_in_block(flat_routes, experts)
    token_ids = jnp.arange(count * chosen, dtype=jnp.int32) // chosen
    source = jnp.full((experts * CAP,), count, jnp.int32).at[target].set(token_ids)

    extra = -(-(experts * CAP) // features)
    stride = count + extra
    table_rows = jnp.zeros((extra * features,), jnp.bfloat16)
    table_rows = table_rows.at[: experts * CAP].set(source.astype(jnp.bfloat16))
    packed = jnp.concatenate([normed, table_rows.reshape(extra, features)], axis=0)
    every = lax.all_gather(packed, ALL, axis=0, tiled=True)

    table_at = jnp.arange(devices, dtype=jnp.int32)[:, None] * stride + count
    table_at = (table_at + jnp.arange(extra, dtype=jnp.int32)[None, :]).reshape(-1)
    tables = jnp.take(every, table_at, axis=0).reshape(devices, -1)
    tables = lax.dynamic_slice_in_dim(
        tables[:, : experts * CAP], owner * holding * CAP, holding * CAP, axis=1
    ).astype(jnp.int32)
    rows = tables + (jnp.arange(devices, dtype=jnp.int32) * stride)[:, None]
    rows = rows.reshape(owners, tok_count, holding, CAP).transpose(2, 1, 0, 3).reshape(-1)
    rows = rows.reshape(holding, -1)
    pieces = math.gcd(holding, PIECES)
    width = holding // pieces
    returned = []
    sums = []
    for piece in range(pieces):
        span = slice(piece * width, (piece + 1) * width)
        picked = jnp.take(every, rows[span].reshape(-1), axis=0, mode="clip")
        picked = picked.reshape(width, tok_count * owners * CAP, features)
        both = jnp.einsum(
            "jrd,jgfd->jrgf", picked, gate_up_weight[span], preferred_element_type=jnp.float32
        )
        hidden = (jax.nn.silu(both[:, :, 0, :]) * both[:, :, 1, :]).astype(jnp.bfloat16)
        partial = jnp.einsum(
            "jrf,jfd->jrd", hidden, down_weight[span], preferred_element_type=jnp.float32
        )
        partial = partial.astype(jnp.bfloat16)
        if sums:
            partial, _ = lax.optimization_barrier((partial, (sums[-1], returned[:-1])))
        sums.append(lax.psum_scatter(partial, "tok", scatter_dimension=1, tiled=True))
        summed = sums[-1].reshape(width, owners, CAP, features).transpose(1, 0, 2, 3)
        summed = summed.reshape(owners, width * CAP, features)
        returned.append(
            lax.all_to_all(summed, ("row", "col"), split_axis=0, concat_axis=0, tiled=True)
        )
    returned = jnp.concatenate(returned, axis=1)
    picked_back = jnp.take(returned.reshape(experts * CAP, features), target, axis=0)
    picked_back = picked_back.reshape(count, chosen, features)
    mixed = jnp.einsum("tk,tkd->td", gates, picked_back.astype(jnp.float32))
    return mixed.astype(jnp.bfloat16)


def solution(mesh):
    in_specs = (
        P(("row", "col", "tok"), None),
        P(),
        P(("row", "col", "tok"), None),
        P(("row", "col", "tok"), None),
        P(("row", "col"), None, "tok", None),
        P(("row", "col"), "tok", None),
    )
    out_specs = P(("row", "col", "tok"), None)
    return jax.shard_map(local, mesh=mesh, in_specs=in_specs, out_specs=out_specs, check_vma=False)
```
